512 devices in a mesh: seq: 64 (over z, y), tp: 8 (over x, core).
Axes of the slice: x: 4, y: 4, z: 16, core: 2. Of those that a mesh axis runs over, the one named last changes fastest.
Arguments:
- cache: bfloat16 [2, 64, 512, 3072], P(None, 'seq', 'tp'), may hold values from -24 to 24
- cache_len: int32 [64], replicated, may hold values from 1 to 512, 16384 in all
- group: bfloat16 [3, 64, 256, 3072], P(None, 'seq', None, 'tp'), may hold values from -24 to 24
- group_req: int32 [64], replicated, may hold values from 0 to 63, each once
- req_order: int32 [64], replicated, may hold values from 0 to 63, each once
Outputs:
- context: bfloat16 [64, 256, 3072], P('seq', None, 'tp')
The draws below stay inside these ranges and needn't reach their ends.
Inputs may be any that keep to these rules, and one draw needn't show every extreme that they name: `group_req`: each request once. `req_order`: each request once.
All inputs are finite; a program needn't handle non-finite values.
Results may differ from the reference program's by a relative error of at most 0.0042.
Values may be sent and summed in bfloat16 or wider, within the bound.
No kernel may reach another device: no remote copies, remote signals or barrier semaphores. Data moves between devices by JAX's collectives and lax.ppermute only.
A program may use at most 64 MiB of HBM per device.

```python
import math
import jax
import jax.numpy as jnp
import numpy as np
from jax import lax

HEADS = 32
HD = 96
MAXLEN = 512
GROUP = 256
REQS = 64


def draw_cache(key, part):
    local_key = jax.random.fold_in(key, 1)
    array_dims = (2, REQS, MAXLEN, HEADS * HD)
    entries = jnp.clip(jax.random.normal(local_key, array_dims, jnp.float32), -4.0, 4.0)
    return entries.astype(jnp.bfloat16)


def draw_group(key, part):
    local_key = jax.random.fold_in(key, 2)
    array_dims = (3, REQS, GROUP, HEADS * HD)
    entries = jnp.clip(jax.random.normal(local_key, array_dims, jnp.float32), -4.0, 4.0)
    return entries.astype(jnp.bfloat16)


def split_up(number_of, total, reach, lean):
    weights = [(1 << 20) // math.isqrt(rank ** lean) + 1 for rank in range(2, number_of + 1)]
    spare, counts = total - reach - (number_of - 1), [1] * (number_of - 1)
    while spare > 0:
        candidates = [i for i in range(number_of - 1) if counts[i] < reach]
        whole, left = sum([weights[i] for i in candidates]), spare
        for i in candidates:
            more = min(reach - counts[i], max(1, left * weights[i] // whole), spare)
            counts[i] = counts[i] + more
            spare = spare - more
    return np.array([reach] + counts)


def uneven(key, number_of, total, most, skew):
    if number_of == 2:
        one = jax.random.randint(key, (), max(1, total - most), min(most, total - 1) + 1)
        return jnp.stack([one, total - one])
    sizes = jnp.asarray(split_up(number_of, total, most, skew), jnp.int32)
    twos = (number_of - 1) // 2
    source_of, receiver = sizes[1:1 + 2 * twos:2], sizes[2:2 + 2 * twos:2]
    slack = jnp.minimum(source_of - 1, most - receiver)
    shifted = jax.random.randint(jax.random.fold_in(key, 1), (twos,), 0, 1 << 20) % (slack + 1)
    sizes = sizes.at[1:1 + 2 * twos:2].set(source_of - shifted).at[2:2 + 2 * twos:2].set(receiver + shifted)
    return sizes[jax.random.permutation(jax.random.fold_in(key, 2), number_of)]


def setup_inputs(seed: int = 0) -> dict:
    splits = jax.random.split(jax.random.key(seed), 6)
    cache = draw_cache(jax.random.fold_in(splits[5], 71), 0)
    cache_len = uneven(splits[1], REQS, REQS * MAXLEN // 2, MAXLEN, 2).astype(jnp.int32)
    group = draw_group(jax.random.fold_in(splits[5], 71), 0)
    group_req = jax.random.permutation(splits[3], REQS).astype(jnp.int32)
    req_order = jax.random.permutation(splits[4], REQS).astype(jnp.int32)
    return {"cache": cache, "cache_len": cache_len, "group": group, "group_req": group_req, "req_order": req_order}


def inverse_table(permutation):
    numbers = jnp.arange(permutation.shape[0], dtype=jnp.int32)
    return jnp.zeros_like(numbers).at[permutation].set(numbers)

def partial_softmax(queries, key_rows, value_rows, allowed, factor):
    scores = jnp.einsum('qhd,khd->hqk', queries.astype(jnp.float32), key_rows.astype(jnp.float32)) * factor
    scores = jnp.where(allowed[None], scores, -jnp.inf)
    row_top = lax.optimization_barrier(jnp.max(scores, axis=-1))
    weights = jnp.exp(scores - row_top[..., None]).astype(jnp.bfloat16)
    weight_sum = lax.optimization_barrier(jnp.sum(weights.astype(jnp.float32), axis=-1))
    weighted = jnp.einsum('hqk,khd->hqd', weights.astype(jnp.float32), value_rows.astype(jnp.float32))
    return (row_top, weight_sum, weighted)

def combine_parts(first_part, second_part):
    top_one, sum_one, mixed_one = first_part
    top_two, sum_two, mixed_two = second_part
    row_top = jnp.maximum(top_one, top_two)
    factor_one = jnp.exp(top_one - row_top)
    factor_two = jnp.exp(top_two - row_top)
    result = (factor_one[..., None] * mixed_one + factor_two[..., None] * mixed_two) / (factor_one * sum_one + factor_two * sum_two)[..., None]
    result = jnp.transpose(result, (1, 0, 2))
    return result.reshape(result.shape[0], -1).astype(jnp.bfloat16)

def reference(cache, cache_len, group, group_req, req_order):
    factor = 1.0 / math.sqrt(HD)
    slot_of = inverse_table(req_order)
    causal = jnp.arange(GROUP)[:, None] >= jnp.arange(GROUP)[None, :]

    def one_device(device):
        request = group_req[device]
        cache_slot = slot_of[request]
        length = cache_len[request]
        queries = group[0, device].reshape(GROUP, HEADS, HD)
        new_keys = group[1, device].reshape(GROUP, HEADS, HD)
        new_values = group[2, device].reshape(GROUP, HEADS, HD)
        old_keys = cache[0, cache_slot].reshape(MAXLEN, HEADS, HD)
        old_values = cache[1, cache_slot].reshape(MAXLEN, HEADS, HD)
        allowed = (jnp.arange(MAXLEN) < length)[None, :]
        cache_part = partial_softmax(queries, old_keys, old_values, allowed, factor)
        group_part = partial_softmax(queries, new_keys, new_values, causal, factor)
        return combine_parts(cache_part, group_part)
    return lax.map(one_device, jnp.arange(REQS, dtype=jnp.int32))
```

```python
import math

import jax
import jax.numpy as jnp
from jax import lax
from jax.sharding import PartitionSpec as P

HD = 96


def inverse_table(permutation):
    numbers = jnp.arange(permutation.shape[0], dtype=jnp.int32)
    matches = permutation[None, :] == numbers[:, None]
    return jnp.sum(jnp.where(matches, numbers[None, :], 0), axis=1)


def partial_part(queries, key_rows, value_rows, keep, factor):
    scores = (
        jnp.einsum("qhd,khd->hqk", queries, key_rows, preferred_element_type=jnp.float32)
        * factor
    )
    scores = jnp.where(keep[None], scores, -jnp.inf)
    row_top = jnp.max(scores, axis=-1)
    weights = jnp.exp(scores - row_top[..., None]).astype(jnp.bfloat16)
    weight_sum = jnp.sum(weights, axis=-1, dtype=jnp.float32)
    weighted = jnp.einsum(
        "hqk,khd->hqd", weights, value_rows, preferred_element_type=jnp.float32
    )
    return (row_top, weight_sum, weighted)


def combine_parts(first_part, second_part):
    top_one, sum_one, mixed_one = first_part
    top_two, sum_two, mixed_two = second_part
    row_top = jnp.maximum(top_one, top_two)
    factor_one = jnp.exp(top_one - row_top)
    factor_two = jnp.exp(top_two - row_top)
    result = (factor_one[..., None] * mixed_one + factor_two[..., None] * mixed_two) / (
        factor_one * sum_one + factor_two * sum_two
    )[..., None]
    result = jnp.transpose(result, (1, 0, 2))
    return result.reshape(result.shape[0], -1).astype(jnp.bfloat16)


def permute_rows(rows, order):
    count = order.shape[0]
    pieces = rows.reshape(count, rows.shape[0] // count, rows.shape[1])
    spread = lax.all_to_all(pieces, "seq", split_axis=0, concat_axis=0, tiled=True)
    ordered = jnp.take(spread, order, axis=0)
    gathered = lax.all_to_all(ordered, "seq", split_axis=0, concat_axis=0, tiled=True)
    return gathered.reshape(rows.shape)


def shards(cache, cache_len, group, group_req, req_order):
    factor = 1.0 / math.sqrt(HD)
    slot_of = inverse_table(req_order)
    index_of = inverse_table(group_req)
    query_source = jnp.take(index_of, req_order)
    cache_source = jnp.take(slot_of, group_req)
    me = lax.axis_index("seq")
    slot_request = jnp.take(req_order, me)
    slot_length = jnp.take(cache_len, slot_request)

    row_count = group.shape[2]
    feature_count = group.shape[3]
    head_count = feature_count // HD
    queries = group[0, 0]
    new_keys = group[1, 0].reshape(row_count, head_count, HD)
    new_values = group[2, 0].reshape(row_count, head_count, HD)

    local = lax.all_to_all(cache[:, 0], "tp", split_axis=2, concat_axis=1, tiled=True)
    position_count = local.shape[1]
    old_keys = local[0].reshape(position_count, head_count, HD)
    old_values = local[1].reshape(position_count, head_count, HD)

    slot_queries = permute_rows(queries, query_source).reshape(row_count, head_count, HD)
    live = (jnp.arange(position_count, dtype=jnp.int32) < slot_length)[None, :]
    top_c, sum_c, mixed_c = partial_part(slot_queries, old_keys, old_values, live, factor)
    packed = jnp.concatenate(
        [
            jnp.transpose(mixed_c, (1, 0, 2)).reshape(row_count, feature_count),
            jnp.transpose(top_c),
            jnp.transpose(sum_c),
        ],
        axis=1,
    )
    back = permute_rows(packed, cache_source)
    cache_part = (
        jnp.transpose(back[:, feature_count : feature_count + head_count]),
        jnp.transpose(back[:, feature_count + head_count :]),
        jnp.transpose(back[:, :feature_count].reshape(row_count, head_count, HD), (1, 0, 2)),
    )

    causal = jnp.arange(row_count, dtype=jnp.int32)[:, None] >= jnp.arange(
        row_count, dtype=jnp.int32
    )[None, :]
    group_part = partial_part(
        queries.reshape(row_count, head_count, HD), new_keys, new_values, causal, factor
    )
    context = combine_parts(cache_part, group_part)
    return context[None]


def solution(mesh):
    in_specs = (P(None, "seq", "tp", None), P(), P(None, "seq", None, "tp"), P(), P())
    out_specs = P("seq", None, "tp")
    return jax.shard_map(shards, mesh=mesh, in_specs=in_specs, out_specs=out_specs, check_vma=False)
```

```python
import math

import jax
import jax.numpy as jnp
from jax import lax
from jax.sharding import PartitionSpec as P

HD = 96


def inverse_table(permutation):
    numbers = jnp.arange(permutation.shape[0], dtype=jnp.int32)
    matches = permutation[None, :] == numbers[:, None]
    return jnp.sum(jnp.where(matches, numbers[None, :], 0), axis=1)


def partial_part(queries, key_rows, value_rows, keep, factor):
    scores = (
        jnp.einsum("qhd,khd->hqk", queries, key_rows, preferred_element_type=jnp.float32)
        * factor
    )
    scores = jnp.where(keep[None], scores, -jnp.inf)
    row_top = jnp.max(scores, axis=-1)
    weights = jnp.exp(scores - row_top[..., None]).astype(jnp.bfloat16)
    weight_sum = jnp.sum(weights, axis=-1, dtype=jnp.float32)
    weighted = jnp.einsum(
        "hqk,khd->hqd", weights, value_rows, preferred_element_type=jnp.float32
    )
    return (row_top, weight_sum, weighted)


def combine_parts(first_part, second_part):
    top_one, sum_one, mixed_one = first_part
    top_two, sum_two, mixed_two = second_part
    row_top = jnp.maximum(top_one, top_two)
    factor_one = jnp.exp(top_one - row_top)
    factor_two = jnp.exp(top_two - row_top)
    result = (factor_one[..., None] * mixed_one + factor_two[..., None] * mixed_two) / (
        factor_one * sum_one + factor_two * sum_two
    )[..., None]
    result = jnp.transpose(result, (1, 0, 2))
    return result.reshape(result.shape[0], -1).astype(jnp.bfloat16)


def shards(cache, cache_len, group, group_req, req_order):
    factor = 1.0 / math.sqrt(HD)
    slot_of = inverse_table(req_order)
    source_slot = jnp.take(slot_of, group_req)
    my_request = jnp.take(group_req, lax.axis_index("seq"))
    length = jnp.take(cache_len, my_request)
    row_count = group.shape[2]
    feature_count = group.shape[3]
    head_count = feature_count // HD
    queries = group[0, 0].reshape(row_count, head_count, HD)
    new_keys = group[1, 0].reshape(row_count, head_count, HD)
    new_values = group[2, 0].reshape(row_count, head_count, HD)

    causal = jnp.arange(row_count, dtype=jnp.int32)[:, None] >= jnp.arange(
        row_count, dtype=jnp.int32
    )[None, :]
    group_part = partial_part(queries, new_keys, new_values, causal, factor)

    seq_count = source_slot.shape[0]
    tp_count = cache.shape[3] // feature_count
    local_positions = cache.shape[2]
    by_position = jnp.transpose(cache[:, 0], (1, 0, 2))
    spread = lax.all_to_all(by_position, "seq", split_axis=0, concat_axis=0, tiled=True)
    ordered = jnp.take(spread, source_slot, axis=0)
    ordered = ordered.reshape(seq_count, 2, tp_count, feature_count)
    ordered = jnp.transpose(ordered, (0, 2, 1, 3))
    moved = lax.all_to_all(
        ordered.reshape(seq_count * tp_count, 2, feature_count),
        ("seq", "tp"),
        split_axis=0,
        concat_axis=0,
        tiled=True,
    )
    row_total = moved.shape[0]
    old_keys = moved[:, 0].reshape(row_total, head_count, HD)
    old_values = moved[:, 1].reshape(row_total, head_count, HD)
    rows = jnp.arange(row_total, dtype=jnp.int32)
    positions = (rows % tp_count) * local_positions + rows // tp_count
    live = (positions < length)[None, :]
    cache_part = partial_part(queries, old_keys, old_values, live, factor)
    context = combine_parts(cache_part, group_part)
    return context[None]


def solution(mesh):
    in_specs = (P(None, "seq", "tp", None), P(), P(None, "seq", None, "tp"), P(), P())
    out_specs = P("seq", None, "tp")
    return jax.shard_map(shards, mesh=mesh, in_specs=in_specs, out_specs=out_specs, check_vma=False)
```

```python
import math

import jax
import jax.numpy as jnp
from jax import lax
from jax.sharding import PartitionSpec as P

HD = 96


def inverse_table(permutation):
    numbers = jnp.arange(permutation.shape[0], dtype=jnp.int32)
    matches = permutation[None, :] == numbers[:, None]
    return jnp.sum(jnp.where(matches, numbers[None, :], 0), axis=1)


def partial_part(queries, key_rows, value_rows, keep, factor):
    scores = (
        jnp.einsum("qhd,khd->hqk", queries, key_rows, preferred_element_type=jnp.float32)
        * factor
    )
    scores = jnp.where(keep[None], scores, -jnp.inf)
    row_top = jnp.max(scores, axis=-1)
    weights = jnp.exp(scores - row_top[..., None]).astype(jnp.bfloat16)
    weight_sum = jnp.sum(weights, axis=-1, dtype=jnp.float32)
    weighted = jnp.einsum(
        "hqk,khd->hqd", weights, value_rows, preferred_element_type=jnp.float32
    )
    return (row_top, weight_sum, weighted)


def combine_parts(first_part, second_part):
    top_one, sum_one, mixed_one = first_part
    top_two, sum_two, mixed_two = second_part
    row_top = jnp.maximum(top_one, top_two)
    factor_one = jnp.exp(top_one - row_top)
    factor_two = jnp.exp(top_two - row_top)
    result = (factor_one[..., None] * mixed_one + factor_two[..., None] * mixed_two) / (
        factor_one * sum_one + factor_two * sum_two
    )[..., None]
    result = jnp.transpose(result, (1, 0, 2))
    return result.reshape(result.shape[0], -1).astype(jnp.bfloat16)


def shards(cache, cache_len, group, group_req, req_order):
    factor = 1.0 / math.sqrt(HD)
    slot_of = inverse_table(req_order)
    source_slot = jnp.take(slot_of, group_req)
    my_request = jnp.take(group_req, lax.axis_index("seq"))
    length = jnp.take(cache_len, my_request)
    row_count = group.shape[2]
    feature_count = group.shape[3]
    head_count = feature_count // HD
    queries = group[0, 0].reshape(row_count, head_count, HD)
    new_keys = group[1, 0].reshape(row_count, head_count, HD)
    new_values = group[2, 0].reshape(row_count, head_count, HD)

    causal = jnp.arange(row_count, dtype=jnp.int32)[:, None] >= jnp.arange(
        row_count, dtype=jnp.int32
    )[None, :]
    group_part = partial_part(queries, new_keys, new_values, causal, factor)

    seq_count = source_slot.shape[0]
    tp_count = cache.shape[3] // feature_count
    local_positions = cache.shape[2]
    pair_rows = cache[:, 0].reshape(2 * local_positions, -1)
    spread = lax.all_to_all(pair_rows, "seq", split_axis=0, concat_axis=0, tiled=True)
    spread = spread.reshape(seq_count, 2, tp_count, feature_count)
    ordered = jnp.take(spread, source_slot, axis=0)
    ordered = jnp.transpose(ordered, (0, 2, 1, 3))
    moved = lax.all_to_all(
        ordered.reshape(seq_count * tp_count, 2, feature_count),
        ("seq", "tp"),
        split_axis=0,
        concat_axis=0,
        tiled=True,
    )
    half = moved.shape[0] // 2
    row_total = half * 2
    old_keys = moved[:half].reshape(row_total, head_count, HD)
    old_values = moved[half:].reshape(row_total, head_count, HD)
    rows = jnp.arange(row_total, dtype=jnp.int32)
    pair = rows % 2
    source_tp = (rows // 2) % tp_count
    source_seq = rows // (2 * tp_count)
    positions = source_tp * local_positions + 2 * source_seq + pair
    live = (positions < length)[None, :]
    cache_part = partial_part(queries, old_keys, old_values, live, factor)
    context = combine_parts(cache_part, group_part)
    return context[None]


def solution(mesh):
    in_specs = (P(None, "seq", "tp", None), P(), P(None, "seq", None, "tp"), P(), P())
    out_specs = P("seq", None, "tp")
    return jax.shard_map(shards, mesh=mesh, in_specs=in_specs, out_specs=out_specs, check_vma=False)
```

```python
import math

import jax
import jax.numpy as jnp
from jax import lax
from jax.sharding import PartitionSpec as P

HD = 96


def inverse_table(permutation):
    numbers = jnp.arange(permutation.shape[0], dtype=jnp.int32)
    matches = permutation[None, :] == numbers[:, None]
    return jnp.sum(jnp.where(matches, numbers[None, :], 0), axis=1)


def partial_part(queries, key_rows, value_rows, keep, factor):
    scores = (
        jnp.einsum("qhd,khd->hqk", queries, key_rows, preferred_element_type=jnp.float32)
        * factor
    )
    scores = jnp.where(keep[None], scores, -jnp.inf)
    row_top = jnp.max(scores, axis=-1)
    weights = jnp.exp(scores - row_top[..., None]).astype(jnp.bfloat16)
    weight_sum = jnp.sum(weights, axis=-1, dtype=jnp.float32)
    weighted = jnp.einsum(
        "hqk,khd->hqd", weights, value_rows, preferred_element_type=jnp.float32
    )
    return (row_top, weight_sum, weighted)


def combine_parts(first_part, second_part):
    top_one, sum_one, mixed_one = first_part
    top_two, sum_two, mixed_two = second_part
    row_top = jnp.maximum(top_one, top_two)
    factor_one = jnp.exp(top_one - row_top)
    factor_two = jnp.exp(top_two - row_top)
    result = (factor_one[..., None] * mixed_one + factor_two[..., None] * mixed_two) / (
        factor_one * sum_one + factor_two * sum_two
    )[..., None]
    result = jnp.transpose(result, (1, 0, 2))
    return result.reshape(result.shape[0], -1).astype(jnp.bfloat16)


def shards(cache, cache_len, group, group_req, req_order):
    factor = 1.0 / math.sqrt(HD)
    slot_of = inverse_table(req_order)
    source_slot = jnp.take(slot_of, group_req)
    my_request = jnp.take(group_req, lax.axis_index("seq"))
    length = jnp.take(cache_len, my_request)
    row_count = group.shape[2]
    feature_count = group.shape[3]
    head_count = feature_count // HD
    queries = group[0, 0].reshape(row_count, head_count, HD)
    new_keys = group[1, 0].reshape(row_count, head_count, HD)
    new_values = group[2, 0].reshape(row_count, head_count, HD)

    causal = jnp.arange(row_count, dtype=jnp.int32)[:, None] >= jnp.arange(
        row_count, dtype=jnp.int32
    )[None, :]
    group_part = partial_part(queries, new_keys, new_values, causal, factor)

    seq_count = source_slot.shape[0]
    tp_count = cache.shape[3] // feature_count
    local_positions = cache.shape[2]
    pair_rows = cache[:, 0].reshape(seq_count, 2, tp_count, feature_count)
    pair_rows = jnp.transpose(pair_rows, (0, 2, 1, 3))
    spread = lax.all_to_all(pair_rows, "seq", split_axis=0, concat_axis=0, tiled=True)
    ordered = jnp.take(spread, source_slot, axis=0)
    moved = lax.all_to_all(
        ordered.reshape(seq_count * tp_count, 2, feature_count),
        ("seq", "tp"),
        split_axis=0,
        concat_axis=0,
        tiled=True,
    )
    half = moved.shape[0] // 2
    row_total = half * 2
    old_keys = moved[:half].reshape(row_total, head_count, HD)
    old_values = moved[half:].reshape(row_total, head_count, HD)
    rows = jnp.arange(row_total, dtype=jnp.int32)
    pair = rows % 2
    source_tp = (rows // 2) % tp_count
    source_seq = rows // (2 * tp_count)
    positions = source_tp * local_positions + 2 * source_seq + pair
    live = (positions < length)[None, :]
    cache_part = partial_part(queries, old_keys, old_values, live, factor)
    context = combine_parts(cache_part, group_part)
    return context[None]


def solution(mesh):
    in_specs = (P(None, "seq", "tp", None), P(), P(None, "seq", None, "tp"), P(), P())
    out_specs = P("seq", None, "tp")
    return jax.shard_map(shards, mesh=mesh, in_specs=in_specs, out_specs=out_specs, check_vma=False)
```

```python
import math

import jax
import jax.numpy as jnp
from jax import lax
from jax.sharding import PartitionSpec as P

HD = 96


def inverse_table(permutation):
    numbers = jnp.arange(permutation.shape[0], dtype=jnp.int32)
    matches = permutation[None, :] == numbers[:, None]
    return jnp.sum(jnp.where(matches, numbers[None, :], 0), axis=1)


def partial_part(queries, key_rows, value_rows, keep, factor):
    scores = (
        jnp.einsum("qhd,khd->hqk", queries, key_rows, preferred_element_type=jnp.float32)
        * factor
    )
    scores = jnp.where(keep[None], scores, -jnp.inf)
    row_top = jnp.max(scores, axis=-1)
    weights = jnp.exp(scores - row_top[..., None]).astype(jnp.bfloat16)
    weight_sum = jnp.sum(weights, axis=-1, dtype=jnp.float32)
    weighted = jnp.einsum(
        "hqk,khd->hqd", weights, value_rows, preferred_element_type=jnp.float32
    )
    return (row_top, weight_sum, weighted)


def combine_parts(first_part, second_part):
    top_one, sum_one, mixed_one = first_part
    top_two, sum_two, mixed_two = second_part
    row_top = jnp.maximum(top_one, top_two)
    factor_one = jnp.exp(top_one - row_top)
    factor_two = jnp.exp(top_two - row_top)
    result = (factor_one[..., None] * mixed_one + factor_two[..., None] * mixed_two) / (
        factor_one * sum_one + factor_two * sum_two
    )[..., None]
    result = jnp.transpose(result, (1, 0, 2))
    return result.reshape(result.shape[0], -1).astype(jnp.bfloat16)


def shards(cache, cache_len, group, group_req, req_order):
    factor = 1.0 / math.sqrt(HD)
    slot_of = inverse_table(req_order)
    source_slot = jnp.take(slot_of, group_req)
    my_request = jnp.take(group_req, lax.axis_index("seq"))
    length = jnp.take(cache_len, my_request)
    row_count = group.shape[2]
    feature_count = group.shape[3]
    head_count = feature_count // HD
    queries = group[0, 0].reshape(row_count, head_count, HD)
    new_keys = group[1, 0].reshape(row_count, head_count, HD)
    new_values = group[2, 0].reshape(row_count, head_count, HD)

    causal = jnp.arange(row_count, dtype=jnp.int32)[:, None] >= jnp.arange(
        row_count, dtype=jnp.int32
    )[None, :]
    group_part = partial_part(queries, new_keys, new_values, causal, factor)

    seq_count = source_slot.shape[0]
    tp_count = cache.shape[3] // feature_count
    local_positions = cache.shape[2]
    pair_rows = cache[:, 0].reshape(seq_count, 2, tp_count, feature_count)
    pair_rows = jnp.transpose(pair_rows, (0, 2, 1, 3))
    spread = lax.all_to_all(pair_rows, "seq", split_axis=0, concat_axis=0, tiled=True)
    ordered = jnp.take(spread, source_slot, axis=0, mode="clip")
    moved = lax.all_to_all(
        ordered.reshape(seq_count * tp_count, 2, feature_count),
        ("seq", "tp"),
        split_axis=0,
        concat_axis=0,
        tiled=True,
    )
    half = moved.shape[0] // 2
    row_total = half * 2
    old_keys = moved[:half].reshape(row_total, head_count, HD)
    old_values = moved[half:].reshape(row_total, head_count, HD)
    rows = jnp.arange(row_total, dtype=jnp.int32)
    pair = rows % 2
    source_tp = (rows // 2) % tp_count
    source_seq = rows // (2 * tp_count)
    positions = source_tp * local_positions + 2 * source_seq + pair
    live = (positions < length)[None, :]
    cache_part = partial_part(queries, old_keys, old_values, live, factor)
    context = combine_parts(cache_part, group_part)
    return context[None]


def solution(mesh):
    in_specs = (P(None, "seq", "tp", None), P(), P(None, "seq", None, "tp"), P(), P())
    out_specs = P("seq", None, "tp")
    return jax.shard_map(shards, mesh=mesh, in_specs=in_specs, out_specs=out_specs, check_vma=False)
```

```python
import math

import jax
import jax.numpy as jnp
from jax import lax
from jax.sharding import PartitionSpec as P

HD = 96


def inverse_table(permutation):
    numbers = jnp.arange(permutation.shape[0], dtype=jnp.int32)
    matches = permutation[None, :] == numbers[:, None]
    return jnp.sum(jnp.where(matches, numbers[None, :], 0), axis=1)


def partial_part(queries, key_rows, value_rows, keep, factor):
    scores = (
        jnp.einsum("qhd,khd->hqk", queries, key_rows, preferred_element_type=jnp.float32)
        * factor
    )
    scores = jnp.where(keep[None], scores, -jnp.inf)
    row_top = jnp.max(scores, axis=-1)
    weights = jnp.exp(scores - row_top[..., None]).astype(jnp.bfloat16)
    weight_sum = jnp.sum(weights, axis=-1, dtype=jnp.float32)
    weighted = jnp.einsum(
        "hqk,khd->hqd", weights, value_rows, preferred_element_type=jnp.float32
    )
    return (row_top, weight_sum, weighted)


def combine_parts(first_part, second_part):
    top_one, sum_one, mixed_one = first_part
    top_two, sum_two, mixed_two = second_part
    row_top = jnp.maximum(top_one, top_two)
    factor_one = jnp.exp(top_one - row_top)
    factor_two = jnp.exp(top_two - row_top)
    result = (factor_one[..., None] * mixed_one + factor_two[..., None] * mixed_two) / (
        factor_one * sum_one + factor_two * sum_two
    )[..., None]
    result = jnp.transpose(result, (1, 0, 2))
    return result.reshape(result.shape[0], -1).astype(jnp.bfloat16)


def shards(cache, cache_len, group, group_req, req_order):
    factor = 1.0 / math.sqrt(HD)
    slot_of = inverse_table(req_order)
    source_slot = jnp.take(slot_of, group_req)
    my_request = jnp.take(group_req, lax.axis_index("seq"))
    length = jnp.take(cache_len, my_request)
    row_count = group.shape[2]
    feature_count = group.shape[3]
    head_count = feature_count // HD
    queries = group[0, 0].reshape(row_count, head_count, HD)
    new_keys = group[1, 0].reshape(row_count, head_count, HD)
    new_values = group[2, 0].reshape(row_count, head_count, HD)

    causal = jnp.arange(row_count, dtype=jnp.int32)[:, None] >= jnp.arange(
        row_count, dtype=jnp.int32
    )[None, :]
    group_part = partial_part(queries, new_keys, new_values, causal, factor)

    seq_count = source_slot.shape[0]
    tp_count = cache.shape[3] // feature_count
    local_positions = cache.shape[2]
    pair_rows = cache[:, 0].reshape(seq_count, 2, tp_count, feature_count)
    pair_rows = jnp.transpose(pair_rows, (0, 2, 1, 3))
    spread = lax.all_to_all(pair_rows, "seq", split_axis=0, concat_axis=0, tiled=True)
    spread = jnp.transpose(spread, (1, 0, 2, 3))
    ordered = jnp.take(spread, source_slot, axis=1, mode="clip")
    moved = lax.all_to_all(
        ordered.reshape(seq_count * tp_count, 2, feature_count),
        ("tp", "seq"),
        split_axis=0,
        concat_axis=0,
        tiled=True,
    )
    moved = moved.reshape(tp_count, seq_count, 2, feature_count)
    half = seq_count // 2
    row_total = tp_count * half * 2
    old_keys = moved[:, :half].reshape(row_total, head_count, HD)
    old_values = moved[:, half:].reshape(row_total, head_count, HD)
    rows = jnp.arange(row_total, dtype=jnp.int32)
    pair = rows % 2
    source_seq = (rows // 2) % half
    source_tp = rows // (2 * half)
    positions = source_tp * local_positions + 2 * source_seq + pair
    live = (positions < length)[None, :]
    cache_part = partial_part(queries, old_keys, old_values, live, factor)
    context = combine_parts(cache_part, group_part)
    return context[None]


def solution(mesh):
    in_specs = (P(None, "seq", "tp", None), P(), P(None, "seq", None, "tp"), P(), P())
    out_specs = P("seq", None, "tp")
    return jax.shard_map(shards, mesh=mesh, in_specs=in_specs, out_specs=out_specs, check_vma=False)
```

```python
import math

import functools

import jax
import jax.numpy as jnp
from jax import lax
from jax.sharding import Mesh
from jax.sharding import PartitionSpec as P

HD = 96


def inverse_table(permutation):
    numbers = jnp.arange(permutation.shape[0], dtype=jnp.int32)
    matches = permutation[None, :] == numbers[:, None]
    return jnp.sum(jnp.where(matches, numbers[None, :], 0), axis=1)


def partial_part(queries, key_rows, value_rows, keep, factor):
    scores = (
        jnp.einsum("qhd,khd->hqk", queries, key_rows, preferred_element_type=jnp.float32)
        * factor
    )
    scores = jnp.where(keep[None], scores, -jnp.inf)
    row_top = jnp.max(scores, axis=-1)
    weights = jnp.exp(scores - row_top[..., None]).astype(jnp.bfloat16)
    weight_sum = jnp.sum(weights, axis=-1, dtype=jnp.float32)
    weighted = jnp.einsum(
        "hqk,khd->hqd", weights, value_rows, preferred_element_type=jnp.float32
    )
    return (row_top, weight_sum, weighted)


def combine_parts(first_part, second_part):
    top_one, sum_one, mixed_one = first_part
    top_two, sum_two, mixed_two = second_part
    row_top = jnp.maximum(top_one, top_two)
    factor_one = jnp.exp(top_one - row_top)
    factor_two = jnp.exp(top_two - row_top)
    result = (factor_one[..., None] * mixed_one + factor_two[..., None] * mixed_two) / (
        factor_one * sum_one + factor_two * sum_two
    )[..., None]
    result = jnp.transpose(result, (1, 0, 2))
    return result.reshape(result.shape[0], -1).astype(jnp.bfloat16)


def shards(inner, cache, cache_len, group, group_req, req_order):
    factor = 1.0 / math.sqrt(HD)
    slot_of = inverse_table(req_order)
    source_slot = jnp.take(slot_of, group_req)
    my_request = jnp.take(group_req, lax.axis_index(("outer", "inner")))
    length = jnp.take(cache_len, my_request)
    row_count = group.shape[2]
    feature_count = group.shape[3]
    head_count = feature_count // HD
    queries = group[0, 0].reshape(row_count, head_count, HD)
    new_keys = group[1, 0].reshape(row_count, head_count, HD)
    new_values = group[2, 0].reshape(row_count, head_count, HD)

    causal = jnp.arange(row_count, dtype=jnp.int32)[:, None] >= jnp.arange(
        row_count, dtype=jnp.int32
    )[None, :]
    group_part = partial_part(queries, new_keys, new_values, causal, factor)

    seq_count = source_slot.shape[0]
    tp_count = cache.shape[3] // feature_count
    local_positions = cache.shape[2]
    pair_rows = cache[:, 0].reshape(seq_count, 2, tp_count, feature_count)
    pair_rows = jnp.transpose(pair_rows, (0, 2, 1, 3))
    spread = lax.all_to_all(
        pair_rows, ("inner", "outer"), split_axis=0, concat_axis=0, tiled=True
    )
    outer = seq_count // inner
    numbers = jnp.arange(seq_count, dtype=jnp.int32)
    needing = (numbers % outer) * inner + numbers // outer
    wanted = jnp.take(source_slot, needing, mode="clip")
    place = (wanted % inner) * outer + wanted // inner
    spread = jnp.transpose(spread, (1, 0, 2, 3))
    ordered = jnp.take(spread, place, axis=1, mode="clip")
    moved = lax.all_to_all(
        ordered.reshape(seq_count * tp_count, 2, feature_count),
        ("tp", "inner", "outer"),
        split_axis=0,
        concat_axis=0,
        tiled=True,
    )
    moved = moved.reshape(tp_count, seq_count, 2, feature_count)
    half = seq_count // 2
    row_total = tp_count * half * 2
    old_keys = moved[:, :half].reshape(row_total, head_count, HD)
    old_values = moved[:, half:].reshape(row_total, head_count, HD)
    rows = jnp.arange(row_total, dtype=jnp.int32)
    pair = rows % 2
    source_seq = (rows // 2) % half
    source_tp = rows // (2 * half)
    positions = source_tp * local_positions + 2 * source_seq + pair
    live = (positions < length)[None, :]
    cache_part = partial_part(queries, old_keys, old_values, live, factor)
    context = combine_parts(cache_part, group_part)
    return context[None]


def solution(mesh):
    seq_devices = mesh.devices[:, 0]
    try:
        inner = len({device.coords[1] for device in seq_devices})
    except AttributeError:
        inner = 1
    if inner < 1 or seq_devices.shape[0] % inner:
        inner = 1
    outer = seq_devices.shape[0] // inner
    split_mesh = Mesh(
        mesh.devices.reshape(outer, inner, mesh.devices.shape[1]), ("outer", "inner", "tp")
    )
    seq = ("outer", "inner")
    in_specs = (P(None, seq, "tp", None), P(), P(None, seq, None, "tp"), P(), P())
    out_specs = P(seq, None, "tp")
    return jax.shard_map(
        functools.partial(shards, inner),
        mesh=split_mesh,
        in_specs=in_specs,
        out_specs=out_specs,
        check_vma=False,
    )
```

```python
import math

import functools

import jax
import jax.numpy as jnp
from jax import lax
from jax.sharding import Mesh
from jax.sharding import PartitionSpec as P

HD = 96


def inverse_table(permutation):
    numbers = jnp.arange(permutation.shape[0], dtype=jnp.int32)
    matches = permutation[None, :] == numbers[:, None]
    return jnp.sum(jnp.where(matches, numbers[None, :], 0), axis=1)


def partial_part(queries, key_rows, value_rows, keep, factor):
    scores = (
        jnp.einsum("qhd,khd->hqk", queries, key_rows, preferred_element_type=jnp.float32)
        * factor
    )
    scores = jnp.where(keep[None], scores, -jnp.inf)
    row_top = jnp.max(scores, axis=-1)
    weights = jnp.exp(scores - row_top[..., None]).astype(jnp.bfloat16)
    weight_sum = jnp.sum(weights, axis=-1, dtype=jnp.float32)
    weighted = jnp.einsum(
        "hqk,khd->hqd", weights, value_rows, preferred_element_type=jnp.float32
    )
    return (row_top, weight_sum, weighted)


def combine_parts(first_part, second_part):
    top_one, sum_one, mixed_one = first_part
    top_two, sum_two, mixed_two = second_part
    row_top = jnp.maximum(top_one, top_two)
    factor_one = jnp.exp(top_one - row_top)
    factor_two = jnp.exp(top_two - row_top)
    result = (factor_one[..., None] * mixed_one + factor_two[..., None] * mixed_two) / (
        factor_one * sum_one + factor_two * sum_two
    )[..., None]
    result = jnp.transpose(result, (1, 0, 2))
    return result.reshape(result.shape[0], -1).astype(jnp.bfloat16)


def shards(inner, cache, cache_len, group, group_req, req_order):
    factor = 1.0 / math.sqrt(HD)
    slot_of = inverse_table(req_order)
    source_slot = jnp.take(slot_of, group_req)
    my_request = jnp.take(group_req, lax.axis_index(("outer", "inner")))
    length = jnp.take(cache_len, my_request)
    row_count = group.shape[2]
    feature_count = group.shape[3]
    head_count = feature_count // HD
    queries = group[0, 0].reshape(row_count, head_count, HD)
    new_keys = group[1, 0].reshape(row_count, head_count, HD)
    new_values = group[2, 0].reshape(row_count, head_count, HD)

    causal = jnp.arange(row_count, dtype=jnp.int32)[:, None] >= jnp.arange(
        row_count, dtype=jnp.int32
    )[None, :]
    group_part = partial_part(queries, new_keys, new_values, causal, factor)

    seq_count = source_slot.shape[0]
    tp_count = cache.shape[3] // feature_count
    local_positions = cache.shape[2]
    pair_rows = cache[:, 0].reshape(seq_count, 2, tp_count, feature_count)
    pair_rows = jnp.transpose(pair_rows, (0, 2, 1, 3))
    spread = lax.all_to_all(
        pair_rows, ("inner", "outer"), split_axis=0, concat_axis=0, tiled=True
    )
    outer = seq_count // inner
    place = (source_slot % inner) * outer + source_slot // inner
    spread = jnp.transpose(spread, (1, 0, 2, 3))
    ordered = jnp.take(spread, place, axis=1, mode="clip")
    moved = lax.all_to_all(
        ordered.reshape(seq_count * tp_count, 2, feature_count),
        ("tp", "outer", "inner"),
        split_axis=0,
        concat_axis=0,
        tiled=True,
    )
    moved = moved.reshape(tp_count, outer, 2, inner // 2, 2, feature_count)
    row_total = seq_count * tp_count
    old_keys = moved[:, :, 0].reshape(row_total, head_count, HD)
    old_values = moved[:, :, 1].reshape(row_total, head_count, HD)
    rows = jnp.arange(row_total, dtype=jnp.int32)
    pair = rows % 2
    low_y = (rows // 2) % (inner // 2)
    source_z = (rows // inner) % outer
    source_tp = rows // (inner * outer)
    positions = source_tp * local_positions + 2 * (low_y * outer + source_z) + pair
    live = (positions < length)[None, :]
    cache_part = partial_part(queries, old_keys, old_values, live, factor)
    context = combine_parts(cache_part, group_part)
    return context[None]


def solution(mesh):
    seq_devices = mesh.devices[:, 0]
    try:
        inner = len({device.coords[1] for device in seq_devices})
    except AttributeError:
        inner = 1
    if inner < 1 or seq_devices.shape[0] % inner:
        inner = 1
    outer = seq_devices.shape[0] // inner
    split_mesh = Mesh(
        mesh.devices.reshape(outer, inner, mesh.devices.shape[1]), ("outer", "inner", "tp")
    )
    seq = ("outer", "inner")
    in_specs = (P(None, seq, "tp", None), P(), P(None, seq, None, "tp"), P(), P())
    out_specs = P(seq, None, "tp")
    return jax.shard_map(
        functools.partial(shards, inner),
        mesh=split_mesh,
        in_specs=in_specs,
        out_specs=out_specs,
        check_vma=False,
    )
```

```python
import math

import jax
import jax.numpy as jnp
from jax import lax
from jax.sharding import PartitionSpec as P

HD = 96


def inverse_table(permutation):
    numbers = jnp.arange(permutation.shape[0], dtype=jnp.int32)
    matches = permutation[None, :] == numbers[:, None]
    return jnp.sum(jnp.where(matches, numbers[None, :], 0), axis=1)


def partial_part(queries, key_rows, value_rows, keep, factor):
    scores = (
        jnp.einsum("qhd,khd->hqk", queries, key_rows, preferred_element_type=jnp.float32)
        * factor
    )
    scores = jnp.where(keep[None], scores, -jnp.inf)
    row_top = jnp.max(scores, axis=-1)
    weights = jnp.exp(scores - row_top[..., None]).astype(jnp.bfloat16)
    weight_sum = jnp.sum(weights, axis=-1, dtype=jnp.float32)
    weighted = jnp.einsum(
        "hqk,khd->hqd", weights, value_rows, preferred_element_type=jnp.float32
    )
    return (row_top, weight_sum, weighted)


def combine_parts(first_part, second_part):
    top_one, sum_one, mixed_one = first_part
    top_two, sum_two, mixed_two = second_part
    row_top = jnp.maximum(top_one, top_two)
    factor_one = jnp.exp(top_one - row_top)
    factor_two = jnp.exp(top_two - row_top)
    result = (factor_one[..., None] * mixed_one + factor_two[..., None] * mixed_two) / (
        factor_one * sum_one + factor_two * sum_two
    )[..., None]
    result = jnp.transpose(result, (1, 0, 2))
    return result.reshape(result.shape[0], -1).astype(jnp.bfloat16)


def shards(cache, cache_len, group, group_req, req_order):
    factor = 1.0 / math.sqrt(HD)
    slot_of = inverse_table(req_order)
    source_slot = jnp.take(slot_of, group_req)
    my_request = jnp.take(group_req, lax.axis_index("seq"))
    length = jnp.take(cache_len, my_request)
    row_count = group.shape[2]
    feature_count = group.shape[3]
    head_count = feature_count // HD
    queries = group[0, 0].reshape(row_count, head_count, HD)
    new_keys = group[1, 0].reshape(row_count, head_count, HD)
    new_values = group[2, 0].reshape(row_count, head_count, HD)

    causal = jnp.arange(row_count, dtype=jnp.int32)[:, None] >= jnp.arange(
        row_count, dtype=jnp.int32
    )[None, :]
    group_part = partial_part(queries, new_keys, new_values, causal, factor)

    seq_count = source_slot.shape[0]
    tp_count = cache.shape[3] // feature_count
    local_positions = cache.shape[2]
    pair_rows = cache[:, 0].reshape(seq_count, 2, tp_count, feature_count)
    pair_rows = jnp.transpose(pair_rows, (0, 2, 1, 3))
    spread = lax.all_to_all(pair_rows, "seq", split_axis=0, concat_axis=0, tiled=True)
    spread = jnp.transpose(spread, (1, 0, 2, 3))
    ordered = jnp.take(spread, source_slot, axis=1, mode="clip")
    moved = lax.all_to_all(
        ordered.reshape(seq_count * tp_count, 2, feature_count),
        ("tp", "seq"),
        split_axis=0,
        concat_axis=0,
        tiled=True,
    )
    moved = moved.reshape(tp_count, seq_count, 2, feature_count)
    half = seq_count // 2
    row_total = tp_count * half * 2
    old_keys = moved[:, :half].reshape(row_total, feature_count)
    old_values = moved[:, half:].reshape(row_total, feature_count)
    rows = jnp.arange(row_total, dtype=jnp.int32)
    pair = rows % 2
    source_seq = (rows // 2) % half
    source_tp = rows // (2 * half)
    positions = source_tp * local_positions + 2 * source_seq + pair
    live = (positions < length)[None, :]
    flat_queries = group[0, 0]
    tops, sums, mixes = [], [], []
    for head in range(head_count):
        columns = slice(head * HD, (head + 1) * HD)
        head_scores = (
            jnp.dot(
                flat_queries[:, columns],
                old_keys[:, columns].T,
                preferred_element_type=jnp.float32,
            )
            * factor
        )
        head_scores = jnp.where(live, head_scores, -jnp.inf)
        head_top = jnp.max(head_scores, axis=-1)
        head_weights = jnp.exp(head_scores - head_top[:, None]).astype(jnp.bfloat16)
        sums.append(jnp.sum(head_weights, axis=-1, dtype=jnp.float32))
        mixes.append(
            jnp.dot(head_weights, old_values[:, columns], preferred_element_type=jnp.float32)
        )
        tops.append(head_top)
    cache_part = (jnp.stack(tops), jnp.stack(sums), jnp.stack(mixes))
    context = combine_parts(cache_part, group_part)
    return context[None]


def solution(mesh):
    in_specs = (P(None, "seq", "tp", None), P(), P(None, "seq", None, "tp"), P(), P())
    out_specs = P("seq", None, "tp")
    return jax.shard_map(shards, mesh=mesh, in_specs=in_specs, out_specs=out_specs, check_vma=False)
```
